1024 devices in a mesh: dp: 16 (over z), fsdp: 32 (over y, x), llm: 2 (over core).
Axes of the slice: x: 4, y: 8, z: 16, core: 2. Of those that a mesh axis runs over, the one named last changes fastest.
Arguments:
- tile_rows: bfloat16 [131072, 768], P(('dp', 'fsdp')), may hold values from -6 to 6
- grad_seq: bfloat16 [262144, 768], P(('dp', 'fsdp')), may hold values from -6 to 6
- visual_pos: int32 [512, 256], P(('dp', 'fsdp')), may hold values from 0 to 511, as said below
- assign: int32 [512, 16], P(('dp', 'fsdp')), may hold values from 0 to 15, each once within a row
- tile_count: int32 [512], P(('dp', 'fsdp')), may hold values from 1 to 4
- kernel: float32 [7, 7, 768], replicated, may hold values from -0.875 to 0.875
- norm_gain: float32 [768], replicated, may hold values from 0.5 to 2
- layer_scale: float32 [768], replicated, may hold values from 0.2 to 2
- weight_in: bfloat16 [768, 1536], P('fsdp', 'llm'), may hold values from -0.21875 to 0.21875
- weight_out: bfloat16 [768, 1536], P('fsdp', 'llm'), may hold values from -0.15625 to 0.15625
Outputs:
- grad_tiles: bfloat16 [131072, 768], P(('dp', 'fsdp'), 'llm')
- grad_weight_in: float32 [12288, 1536], P(('dp', 'fsdp'), 'llm')
- grad_weight_out: float32 [12288, 1536], P(('dp', 'fsdp'), 'llm')
The draws below stay inside these ranges and needn't reach their ends.
Inputs may be any that keep to these rules, and one draw needn't show every extreme that they name: `visual_pos`: each row is strictly increasing. `assign`: each row names every group once.
All inputs are finite; a program needn't handle non-finite values.
Results may differ from the reference program's by a relative error of at most 0.015.
Values may be sent and summed in bfloat16 or wider, within the bound.
No kernel may reach another device: no remote copies, remote signals or barrier semaphores. Data moves between devices by JAX's collectives and lax.ppermute only.
A program may use at most 32 MiB of HBM per device.

```python
import math
import jax
import jax.numpy as jnp
from jax import lax

C = 768
HID = 1536
KS = 7
SIDE = 8
TILES_DEV = 4
ACCUM = 64
ROWS_DEV = 256
SEQ_DEV = 512
TOKENS = 131072
N_DP = 16
N_FSDP = 32


def draw_visual_pos(key, part):
    devices_all = TOKENS // ROWS_DEV
    scores = jax.random.randint(key, (devices_all, SEQ_DEV), 0, 131072) * SEQ_DEV + jnp.arange(SEQ_DEV)[None, :]
    ranking = jnp.argsort(scores, axis=1)
    return jnp.sort(ranking[:, :ROWS_DEV], axis=1).astype(jnp.int32)


def set_ends(result, own_key, smallest, high):
    longest = result.shape.index(max(result.shape))
    spots = []
    for shift in (0, 1):
        where = [jax.random.randint(jax.random.fold_in(own_key, axis), (), 0, length) for axis, length in enumerate(result.shape)]
        where[longest] = (where[longest] + shift) % result.shape[longest]
        spots.append(tuple(where))
    return result.at[spots[0]].set(smallest).at[spots[1]].set(high)


def levels(rng, extent, cuts, smallest, top_value):
    loudness, own = 1.0, jax.random.fold_in(rng, 6)
    for dim, blocks in cuts:
        draws = jnp.exp(jax.random.uniform(jax.random.fold_in(own, dim), (blocks,), jnp.float32, smallest / len(cuts), top_value / len(cuts)))
        loudness = loudness * jnp.repeat(draws, extent[dim] // blocks).reshape([-1 if axis == dim else 1 for axis in range(len(extent))])
    return loudness


def bell_draw(rng, extent, width, limit, split=(), kind=jnp.bfloat16):
    level = levels(rng, extent, split, -0.22, 0.18) if split else 1.0
    array = jax.random.normal(rng, extent, jnp.float32) * width * level
    return jnp.minimum(jnp.maximum(array, -limit), limit).astype(kind)


def setup_inputs(seed: int = 0) -> dict:
    key_list = jax.random.split(jax.random.key(seed), 11)
    tile_rows = bell_draw(key_list[0], (TOKENS, C), 1.0, 6.0, ((0, 512),))
    grad_seq = bell_draw(key_list[1], (N_DP * N_FSDP * SEQ_DEV, C), 1.0, 6.0, ((0, 512),))
    visual_pos = draw_visual_pos(jax.random.fold_in(key_list[10], 71), 0)
    assign = jax.vmap(lambda own: jax.random.permutation(own, N_DP))(jax.random.split(key_list[3], (N_DP * N_FSDP))).reshape((N_DP * N_FSDP, N_DP)).astype(jnp.int32)
    tile_count = set_ends(jax.random.randint(key_list[4], (N_DP * N_FSDP,), 1, TILES_DEV + 1), jax.random.fold_in(key_list[4], 1), 1, TILES_DEV).astype(jnp.int32)
    kernel = bell_draw(key_list[5], (KS, KS, C), (KS * KS) ** -0.5, 0.875, (), jnp.float32)
    norm_gain = jnp.clip(jnp.exp(jax.random.uniform(key_list[6], (C,), jnp.float32, math.log(0.5), math.log(2.0))), 0.5, 2.0)
    layer_scale = jnp.clip(jnp.exp(jax.random.uniform(key_list[7], (C,), jnp.float32, math.log(0.2), math.log(2.0))), 0.2, 2.0)
    weight_in = bell_draw(key_list[8], (C, HID), C ** -0.5, 0.21875, ((0, 32), (1, 2)))
    weight_out = bell_draw(key_list[9], (C, HID), HID ** -0.5, 0.15625, ((0, 32), (1, 2)))
    return {"tile_rows": tile_rows, "grad_seq": grad_seq, "visual_pos": visual_pos, "assign": assign, "tile_count": tile_count, "kernel": kernel, "norm_gain": norm_gain, "layer_scale": layer_scale, "weight_in": weight_in, "weight_out": weight_out}


def depthwise(images, kernel):
    return lax.conv_general_dilated(images, kernel[:, :, None, :], (1, 1), 'SAME', dimension_numbers=('NHWC', 'HWIO', 'NHWC'), feature_group_count=images.shape[3], precision=lax.Precision.HIGHEST)

def gelu_parts(hidden_in):
    cumulative = 0.5 * (1.0 + lax.erf(hidden_in * 0.7071067811865476))
    density = jnp.exp(-0.5 * hidden_in * hidden_in) * 0.3989422804014327
    return (hidden_in * cumulative, cumulative + hidden_in * density)

def partial_sums(left, right):
    terms = jnp.einsum('src,srh->sch', left.reshape(N_FSDP, ROWS_DEV, -1).astype(jnp.float32), right.reshape(N_FSDP, ROWS_DEV, -1).astype(jnp.float32))
    rounded = lax.optimization_barrier(terms.astype(jnp.bfloat16))
    return lax.optimization_barrier(jnp.sum(rounded.astype(jnp.float32), axis=0)) / ACCUM

def reference(tile_rows, grad_seq, visual_pos, assign, tile_count, kernel, norm_gain, layer_scale, weight_in, weight_out):
    groups = N_DP
    shards = N_FSDP
    block_rows = ROWS_DEV // groups
    visual = jnp.take_along_axis(grad_seq.reshape(groups * shards, SEQ_DEV, C), visual_pos[:, :, None], axis=1)
    blocks = visual.reshape(groups, shards, groups, block_rows, C)
    chosen = jnp.take_along_axis(blocks, assign.reshape(groups, shards, groups, 1, 1), axis=2)
    arrived = jnp.transpose(chosen, (2, 1, 0, 3, 4)).reshape(groups, shards, ROWS_DEV, C)
    present = (jnp.arange(ROWS_DEV) // (SIDE * SIDE))[None, :] < tile_count[:, None]
    present = present.reshape(groups, shards, ROWS_DEV, 1)
    grad_out = jnp.where(present, arrived, jnp.zeros_like(arrived))
    inputs = tile_rows.reshape(groups, shards, ROWS_DEV, C)

    def group_backward(pieces):
        x_group, dy_group = pieces
        x_rows = x_group.reshape(shards * ROWS_DEV, C)
        dy_rows = dy_group.reshape(shards * ROWS_DEV, C)
        mixed = depthwise(x_rows.astype(jnp.float32).reshape(-1, SIDE, SIDE, C), kernel).reshape(-1, C)
        row_mean = lax.optimization_barrier(jnp.mean(mixed, axis=1, keepdims=True))
        centred = mixed - row_mean
        inv_std = lax.rsqrt(lax.optimization_barrier(jnp.mean(centred * centred, axis=1, keepdims=True)) + 1e-06)
        unit = centred * inv_std
        normed = (unit * norm_gain).astype(jnp.bfloat16)
        hidden_in = jnp.dot(normed, weight_in, preferred_element_type=jnp.float32)
        activated, slope = gelu_parts(hidden_in)
        hidden = activated.astype(jnp.bfloat16)
        scaled = (dy_rows.astype(jnp.float32) * layer_scale).astype(jnp.bfloat16)
        grad_hidden = jnp.dot(scaled, weight_out, preferred_element_type=jnp.float32)
        grad_pre = (grad_hidden * slope).astype(jnp.bfloat16)
        grad_in = partial_sums(normed, grad_pre)
        grad_outw = partial_sums(scaled, hidden)
        grad_normed = lax.dot_general(grad_pre, weight_in, (((1,), (1,)), ((), ())), preferred_element_type=jnp.float32)
        grad_unit = grad_normed * norm_gain
        mean_grad = lax.optimization_barrier(jnp.mean(grad_unit, axis=1, keepdims=True))
        mean_cross = lax.optimization_barrier(jnp.mean(grad_unit * unit, axis=1, keepdims=True))
        grad_mixed = inv_std * (grad_unit - mean_grad - unit * mean_cross)
        backward = depthwise(grad_mixed.reshape(-1, SIDE, SIDE, C), kernel[::-1, ::-1]).reshape(-1, C)
        grad_tiles = (dy_rows.astype(jnp.float32) + backward).astype(jnp.bfloat16)
        return (grad_tiles, grad_in, grad_outw)
    grad_tiles, grad_in, grad_outw = lax.map(group_backward, (inputs, grad_out))
    return (grad_tiles.reshape(groups * shards * ROWS_DEV, C), grad_in.reshape(groups * C, HID), grad_outw.reshape(groups * C, HID))
```

```python
import jax
import jax.numpy as jnp
from jax import lax
from jax.sharding import PartitionSpec as P

SIDE = 8
ACCUM = 64


def depthwise(images, kernel):
    return lax.conv_general_dilated(
        images,
        kernel[:, :, None, :],
        (1, 1),
        "SAME",
        dimension_numbers=("NHWC", "HWIO", "NHWC"),
        feature_group_count=images.shape[3],
        precision=lax.Precision.HIGHEST,
    )


def gelu_parts(hidden_in):
    cumulative = 0.5 * (1.0 + lax.erf(hidden_in * 0.7071067811865476))
    density = jnp.exp(-0.5 * hidden_in * hidden_in) * 0.3989422804014327
    return (hidden_in * cumulative, cumulative + hidden_in * density)


SWAP = [(0, 1), (1, 0)]


def body(
    tile_rows,
    grad_seq,
    visual_pos,
    assign,
    tile_count,
    kernel,
    norm_gain,
    layer_scale,
    weight_in,
    weight_out,
):
    groups = lax.axis_size("dp")
    shards = lax.axis_size("fsdp")
    row_count = tile_rows.shape[0]
    channels = tile_rows.shape[1]
    block_rows = row_count // groups
    half_width = channels // lax.axis_size("llm")
    core_index = lax.axis_index("llm")

    visual = jnp.take(grad_seq, visual_pos[0], axis=0)
    outgoing = jnp.take(visual.reshape(groups, block_rows, channels), assign[0], axis=0).reshape(
        row_count, channels
    )
    out_half = lax.dynamic_slice_in_dim(outgoing, core_index * half_width, half_width, 1)
    arrived_half = lax.all_to_all(out_half, "dp", split_axis=0, concat_axis=0, tiled=True)
    present = jnp.arange(row_count) // (SIDE * SIDE) < tile_count[0]
    mine_half = jnp.where(present[:, None], arrived_half, jnp.zeros_like(arrived_half))
    other_half = lax.ppermute(mine_half, "llm", SWAP)
    first = jnp.where(core_index == 0, mine_half, other_half)
    second = jnp.where(core_index == 0, other_half, mine_half)
    grad_out = jnp.concatenate([first, second], axis=1)

    hid = weight_in.shape[1]
    both = jnp.concatenate([weight_in, weight_out], axis=1)
    both_tiled = jnp.broadcast_to(both[None], (shards,) + both.shape)
    both_full = lax.all_to_all(both_tiled, "fsdp", split_axis=0, concat_axis=0).reshape(
        shards * both.shape[0], both.shape[1]
    )
    w_in_full = both_full[:, :hid]
    w_out_full = both_full[:, hid:]

    mixed = depthwise(
        tile_rows.astype(jnp.float32).reshape(-1, SIDE, SIDE, channels), kernel
    ).reshape(row_count, channels)
    row_mean = jnp.mean(mixed, axis=1, keepdims=True)
    centred = mixed - row_mean
    inv_std = lax.rsqrt(jnp.mean(centred * centred, axis=1, keepdims=True) + 1e-06)
    unit = centred * inv_std
    normed = (unit * norm_gain).astype(jnp.bfloat16)
    hidden_in = jnp.dot(normed, w_in_full, preferred_element_type=jnp.float32)
    activated, slope = gelu_parts(hidden_in)
    hidden = activated.astype(jnp.bfloat16)
    scaled = (grad_out.astype(jnp.float32) * layer_scale).astype(jnp.bfloat16)
    grad_hidden = jnp.dot(scaled, w_out_full, preferred_element_type=jnp.float32)
    grad_pre = (grad_hidden * slope).astype(jnp.bfloat16)

    term_in = lax.dot_general(
        normed, grad_pre, (((0,), (0,)), ((), ())), preferred_element_type=jnp.float32
    )
    term_out = lax.dot_general(
        scaled, hidden, (((0,), (0,)), ((), ())), preferred_element_type=jnp.float32
    )
    terms = jnp.concatenate([term_in, term_out], axis=1).astype(jnp.bfloat16)
    terms = terms.reshape(shards, channels // shards, 2 * hid)
    gathered = lax.all_to_all(terms, "fsdp", split_axis=0, concat_axis=0)
    totals = jnp.sum(gathered.astype(jnp.float32), axis=0)
    grad_in = totals[:, :hid] / ACCUM
    grad_outw = totals[:, hid:] / ACCUM

    grad_part = lax.dot_general(
        grad_pre, w_in_full, (((1,), (1,)), ((), ())), preferred_element_type=jnp.float32
    )
    part_lo = grad_part[:, :half_width]
    part_hi = grad_part[:, half_width:]
    keep = jnp.where(core_index == 0, part_lo, part_hi)
    send = jnp.where(core_index == 0, part_hi, part_lo).astype(jnp.bfloat16)
    received = lax.ppermute(send, "llm", SWAP)
    grad_normed = keep + received.astype(jnp.float32)
    gain_half = lax.dynamic_slice_in_dim(norm_gain, core_index * half_width, half_width, 0)
    unit_half = lax.dynamic_slice_in_dim(unit, core_index * half_width, half_width, 1)
    grad_unit = grad_normed * gain_half
    sums = jnp.stack(
        [jnp.sum(grad_unit, axis=1), jnp.sum(grad_unit * unit_half, axis=1)], axis=1
    )
    sums = sums + lax.ppermute(sums, "llm", SWAP)
    mean_grad = sums[:, 0:1] / channels
    mean_cross = sums[:, 1:2] / channels
    grad_mixed = inv_std * (grad_unit - mean_grad - unit_half * mean_cross)
    kernel_half = lax.dynamic_slice_in_dim(kernel, core_index * half_width, half_width, 2)
    backward_half = depthwise(
        grad_mixed.reshape(-1, SIDE, SIDE, half_width), kernel_half[::-1, ::-1]
    ).reshape(row_count, half_width)
    grad_tiles = (mine_half.astype(jnp.float32) + backward_half).astype(jnp.bfloat16)
    return (grad_tiles, grad_in, grad_outw)


def solution(mesh):
    in_specs = (
        P(("dp", "fsdp"), None),
        P(("dp", "fsdp"), None),
        P(("dp", "fsdp"), None),
        P(("dp", "fsdp"), None),
        P(("dp", "fsdp")),
        P(),
        P(),
        P(),
        P("fsdp", "llm"),
        P("fsdp", "llm"),
    )
    out_specs = (P(("dp", "fsdp"), "llm"), P(("dp", "fsdp"), "llm"), P(("dp", "fsdp"), "llm"))
    return jax.shard_map(body, mesh=mesh, in_specs=in_specs, out_specs=out_specs, check_vma=False)
```

```python
import functools

import jax
import jax.numpy as jnp
from jax import lax
from jax.sharding import PartitionSpec as P

SIDE = 8
ACCUM = 64


def depthwise(images, kernel):
    return lax.conv_general_dilated(
        images,
        kernel[:, :, None, :],
        (1, 1),
        "SAME",
        dimension_numbers=("NHWC", "HWIO", "NHWC"),
        feature_group_count=images.shape[3],
        precision=lax.Precision.HIGHEST,
    )


def gelu_parts(hidden_in):
    cumulative = 0.5 * (1.0 + lax.erf(hidden_in * 0.7071067811865476))
    density = jnp.exp(-0.5 * hidden_in * hidden_in) * 0.3989422804014327
    return (hidden_in * cumulative, cumulative + hidden_in * density)


def ring_perm(size, width, step_y, step_x):
    height = size // width
    return [
        (y * width + x, ((y + step_y) % height) * width + (x + step_x) % width)
        for y in range(height)
        for x in range(width)
    ]


def ring_gather(block, width):
    size = lax.axis_size("fsdp")
    height = size // width
    f = lax.axis_index("fsdp")
    y, x = f // width, f % width
    rows = block.shape[0]

    def send(value, step_y, step_x):
        return lax.ppermute(value, "fsdp", ring_perm(size, width, step_y, step_x))

    rel = [None] * width
    rel[0] = block
    right, left = block, block
    for k in range(1, width // 2 + 1):
        if 2 * k == width:
            half = rows // 2
            low = send(right[:half], 0, 1)
            high = send(left[half:], 0, -1)
            rel[k] = jnp.concatenate([low, high], axis=0)
        else:
            right = send(right, 0, 1)
            left = send(left, 0, -1)
            rel[width - k] = right
            rel[k] = left
    xblock = jnp.stack(rel)
    rely = [None] * height
    rely[0] = xblock
    up, down = xblock, xblock
    for m in range(1, height // 2 + 1):
        if 2 * m == height:
            half = rows // 2
            low = send(up[:, :half], -1, 0)
            high = send(down[:, half:], 1, 0)
            rely[m] = jnp.concatenate([low, high], axis=1)
        else:
            up = send(up, -1, 0)
            down = send(down, 1, 0)
            rely[m] = up
            rely[height - m] = down
    full = jnp.stack(rely)
    full = jnp.roll(full, (y, x), axis=(0, 1))
    return full.reshape(size * rows, block.shape[1])


SWAP = [(0, 1), (1, 0)]


def body(
    fsdp_x,
    tile_rows,
    grad_seq,
    visual_pos,
    assign,
    tile_count,
    kernel,
    norm_gain,
    layer_scale,
    weight_in,
    weight_out,
):
    groups = lax.axis_size("dp")
    shards = lax.axis_size("fsdp")
    row_count = tile_rows.shape[0]
    channels = tile_rows.shape[1]
    block_rows = row_count // groups
    half_width = channels // lax.axis_size("llm")
    core_index = lax.axis_index("llm")

    visual = jnp.take(grad_seq, visual_pos[0], axis=0)
    outgoing = jnp.take(visual.reshape(groups, block_rows, channels), assign[0], axis=0).reshape(
        row_count, channels
    )
    out_half = lax.dynamic_slice_in_dim(outgoing, core_index * half_width, half_width, 1)
    arrived_half = lax.all_to_all(out_half, "dp", split_axis=0, concat_axis=0, tiled=True)
    present = jnp.arange(row_count) // (SIDE * SIDE) < tile_count[0]
    mine_half = jnp.where(present[:, None], arrived_half, jnp.zeros_like(arrived_half))
    other_half = lax.ppermute(mine_half, "llm", SWAP)
    first = jnp.where(core_index == 0, mine_half, other_half)
    second = jnp.where(core_index == 0, other_half, mine_half)
    grad_out = jnp.concatenate([first, second], axis=1)

    hid = weight_in.shape[1]
    both = jnp.concatenate([weight_in, weight_out], axis=1)
    both_full = ring_gather(both, fsdp_x)
    w_in_full = both_full[:, :hid]
    w_out_full = both_full[:, hid:]

    mixed = depthwise(
        tile_rows.astype(jnp.float32).reshape(-1, SIDE, SIDE, channels), kernel
    ).reshape(row_count, channels)
    row_mean = jnp.mean(mixed, axis=1, keepdims=True)
    centred = mixed - row_mean
    inv_std = lax.rsqrt(jnp.mean(centred * centred, axis=1, keepdims=True) + 1e-06)
    unit = centred * inv_std
    normed = (unit * norm_gain).astype(jnp.bfloat16)
    hidden_in = jnp.dot(normed, w_in_full, preferred_element_type=jnp.float32)
    activated, slope = gelu_parts(hidden_in)
    hidden = activated.astype(jnp.bfloat16)
    scaled = (grad_out.astype(jnp.float32) * layer_scale).astype(jnp.bfloat16)
    grad_hidden = jnp.dot(scaled, w_out_full, preferred_element_type=jnp.float32)
    grad_pre = (grad_hidden * slope).astype(jnp.bfloat16)

    term_in = lax.dot_general(
        normed, grad_pre, (((0,), (0,)), ((), ())), preferred_element_type=jnp.float32
    )
    term_out = lax.dot_general(
        scaled, hidden, (((0,), (0,)), ((), ())), preferred_element_type=jnp.float32
    )
    terms = jnp.concatenate([term_in, term_out], axis=1).astype(jnp.bfloat16)
    terms = terms.reshape(shards, channels // shards, 2 * hid)
    gathered = lax.all_to_all(terms, "fsdp", split_axis=0, concat_axis=0)
    totals = jnp.sum(gathered.astype(jnp.float32), axis=0)
    grad_in = totals[:, :hid] / ACCUM
    grad_outw = totals[:, hid:] / ACCUM

    grad_part = lax.dot_general(
        grad_pre, w_in_full, (((1,), (1,)), ((), ())), preferred_element_type=jnp.float32
    )
    part_lo = grad_part[:, :half_width]
    part_hi = grad_part[:, half_width:]
    keep = jnp.where(core_index == 0, part_lo, part_hi)
    send = jnp.where(core_index == 0, part_hi, part_lo).astype(jnp.bfloat16)
    received = lax.ppermute(send, "llm", SWAP)
    grad_normed = keep + received.astype(jnp.float32)
    gain_half = lax.dynamic_slice_in_dim(norm_gain, core_index * half_width, half_width, 0)
    unit_half = lax.dynamic_slice_in_dim(unit, core_index * half_width, half_width, 1)
    grad_unit = grad_normed * gain_half
    sums = jnp.stack(
        [jnp.sum(grad_unit, axis=1), jnp.sum(grad_unit * unit_half, axis=1)], axis=1
    )
    sums = sums + lax.ppermute(sums, "llm", SWAP)
    mean_grad = sums[:, 0:1] / channels
    mean_cross = sums[:, 1:2] / channels
    grad_mixed = inv_std * (grad_unit - mean_grad - unit_half * mean_cross)
    kernel_half = lax.dynamic_slice_in_dim(kernel, core_index * half_width, half_width, 2)
    backward_half = depthwise(
        grad_mixed.reshape(-1, SIDE, SIDE, half_width), kernel_half[::-1, ::-1]
    ).reshape(row_count, half_width)
    grad_tiles = (mine_half.astype(jnp.float32) + backward_half).astype(jnp.bfloat16)
    return (grad_tiles, grad_in, grad_outw)


def x_width(mesh):
    group = mesh.devices[0, :, 0]
    try:
        return len({d.coords[0] for d in group})
    except (AttributeError, TypeError, IndexError):
        return 4


def solution(mesh):
    in_specs = (
        P(("dp", "fsdp"), None),
        P(("dp", "fsdp"), None),
        P(("dp", "fsdp"), None),
        P(("dp", "fsdp"), None),
        P(("dp", "fsdp")),
        P(),
        P(),
        P(),
        P("fsdp", "llm"),
        P("fsdp", "llm"),
    )
    out_specs = (P(("dp", "fsdp"), "llm"), P(("dp", "fsdp"), "llm"), P(("dp", "fsdp"), "llm"))
    return jax.shard_map(functools.partial(body, x_width(mesh)), mesh=mesh, in_specs=in_specs, out_specs=out_specs, check_vma=False)
```

```python
import jax
import jax.numpy as jnp
from jax import lax
from jax.sharding import PartitionSpec as P

SIDE = 8
ACCUM = 64


def depthwise(images, kernel):
    return lax.conv_general_dilated(
        images,
        kernel[:, :, None, :],
        (1, 1),
        "SAME",
        dimension_numbers=("NHWC", "HWIO", "NHWC"),
        feature_group_count=images.shape[3],
        precision=lax.Precision.HIGHEST,
    )


def gelu_parts(hidden_in):
    cumulative = 0.5 * (1.0 + lax.erf(hidden_in * 0.7071067811865476))
    density = jnp.exp(-0.5 * hidden_in * hidden_in) * 0.3989422804014327
    return (hidden_in * cumulative, cumulative + hidden_in * density)


SWAP = [(0, 1), (1, 0)]


def body(
    tile_rows,
    grad_seq,
    visual_pos,
    assign,
    tile_count,
    kernel,
    norm_gain,
    layer_scale,
    weight_in,
    weight_out,
):
    groups = lax.axis_size("dp")
    height = lax.axis_size("fy")
    width = lax.axis_size("fx")
    shards = height * width
    row_count = tile_rows.shape[0]
    channels = tile_rows.shape[1]
    block_rows = row_count // groups
    half_width = channels // lax.axis_size("llm")
    core_index = lax.axis_index("llm")

    visual = jnp.take(grad_seq, visual_pos[0], axis=0)
    outgoing = jnp.take(visual.reshape(groups, block_rows, channels), assign[0], axis=0).reshape(
        row_count, channels
    )
    out_half = lax.dynamic_slice_in_dim(outgoing, core_index * half_width, half_width, 1)
    arrived_half = lax.all_to_all(out_half, "dp", split_axis=0, concat_axis=0, tiled=True)
    present = jnp.arange(row_count) // (SIDE * SIDE) < tile_count[0]
    mine_half = jnp.where(present[:, None], arrived_half, jnp.zeros_like(arrived_half))
    other_half = lax.ppermute(mine_half, "llm", SWAP)
    first = jnp.where(core_index == 0, mine_half, other_half)
    second = jnp.where(core_index == 0, other_half, mine_half)
    grad_out = jnp.concatenate([first, second], axis=1)

    hid = weight_in.shape[1]
    both = jnp.concatenate([weight_in, weight_out], axis=1)
    y_tiled = jnp.broadcast_to(both[None], (height,) + both.shape)
    y_block = lax.all_to_all(y_tiled, "fy", split_axis=0, concat_axis=0)
    x_tiled = jnp.broadcast_to(y_block[:, None], (height, width) + both.shape)
    both_full = lax.all_to_all(x_tiled, "fx", split_axis=1, concat_axis=1, tiled=True).reshape(
        shards * both.shape[0], both.shape[1]
    )
    w_in_full = both_full[:, :hid]
    w_out_full = both_full[:, hid:]

    mixed = depthwise(
        tile_rows.astype(jnp.float32).reshape(-1, SIDE, SIDE, channels), kernel
    ).reshape(row_count, channels)
    row_mean = jnp.mean(mixed, axis=1, keepdims=True)
    centred = mixed - row_mean
    inv_std = lax.rsqrt(jnp.mean(centred * centred, axis=1, keepdims=True) + 1e-06)
    unit = centred * inv_std
    normed = (unit * norm_gain).astype(jnp.bfloat16)
    hidden_in = jnp.dot(normed, w_in_full, preferred_element_type=jnp.float32)
    activated, slope = gelu_parts(hidden_in)
    hidden = activated.astype(jnp.bfloat16)
    scaled = (grad_out.astype(jnp.float32) * layer_scale).astype(jnp.bfloat16)
    grad_hidden = jnp.dot(scaled, w_out_full, preferred_element_type=jnp.float32)
    grad_pre = (grad_hidden * slope).astype(jnp.bfloat16)

    term_in = lax.dot_general(
        normed, grad_pre, (((0,), (0,)), ((), ())), preferred_element_type=jnp.float32
    )
    term_out = lax.dot_general(
        scaled, hidden, (((0,), (0,)), ((), ())), preferred_element_type=jnp.float32
    )
    terms = jnp.concatenate([term_in, term_out], axis=1).astype(jnp.bfloat16)
    terms = terms.reshape(height, width, channels // shards, 2 * hid)
    x_parts = lax.all_to_all(terms, "fx", split_axis=1, concat_axis=1, tiled=True)
    x_sums = jnp.sum(x_parts.astype(jnp.float32), axis=1).astype(jnp.bfloat16)
    y_parts = lax.all_to_all(x_sums, "fy", split_axis=0, concat_axis=0, tiled=True)
    totals = jnp.sum(y_parts.astype(jnp.float32), axis=0)
    grad_in = totals[:, :hid] / ACCUM
    grad_outw = totals[:, hid:] / ACCUM

    grad_part = lax.dot_general(
        grad_pre, w_in_full, (((1,), (1,)), ((), ())), preferred_element_type=jnp.float32
    )
    part_lo = grad_part[:, :half_width]
    part_hi = grad_part[:, half_width:]
    keep = jnp.where(core_index == 0, part_lo, part_hi)
    send = jnp.where(core_index == 0, part_hi, part_lo).astype(jnp.bfloat16)
    received = lax.ppermute(send, "llm", SWAP)
    grad_normed = keep + received.astype(jnp.float32)
    gain_half = lax.dynamic_slice_in_dim(norm_gain, core_index * half_width, half_width, 0)
    unit_half = lax.dynamic_slice_in_dim(unit, core_index * half_width, half_width, 1)
    grad_unit = grad_normed * gain_half
    sums = jnp.stack(
        [jnp.sum(grad_unit, axis=1), jnp.sum(grad_unit * unit_half, axis=1)], axis=1
    )
    sums = sums + lax.ppermute(sums, "llm", SWAP)
    mean_grad = sums[:, 0:1] / channels
    mean_cross = sums[:, 1:2] / channels
    grad_mixed = inv_std * (grad_unit - mean_grad - unit_half * mean_cross)
    kernel_half = lax.dynamic_slice_in_dim(kernel, core_index * half_width, half_width, 2)
    backward_half = depthwise(
        grad_mixed.reshape(-1, SIDE, SIDE, half_width), kernel_half[::-1, ::-1]
    ).reshape(row_count, half_width)
    grad_tiles = (mine_half.astype(jnp.float32) + backward_half).astype(jnp.bfloat16)
    return (grad_tiles, grad_in, grad_outw)


def x_width(mesh):
    group = mesh.devices[0, :, 0]
    try:
        return len({d.coords[0] for d in group})
    except (AttributeError, TypeError, IndexError):
        return 4


def solution(mesh):
    dp, fsdp, llm = mesh.devices.shape
    width = x_width(mesh)
    split = jax.sharding.Mesh(
        mesh.devices.reshape(dp, fsdp // width, width, llm), ("dp", "fy", "fx", "llm")
    )
    rows = ("dp", "fy", "fx")
    in_specs = (
        P(rows, None),
        P(rows, None),
        P(rows, None),
        P(rows, None),
        P(rows),
        P(),
        P(),
        P(),
        P(("fy", "fx"), "llm"),
        P(("fy", "fx"), "llm"),
    )
    out_specs = (P(rows, "llm"), P(rows, "llm"), P(rows, "llm"))
    return jax.shard_map(body, mesh=split, in_specs=in_specs, out_specs=out_specs, check_vma=False)
```

```python
import jax
import jax.numpy as jnp
from jax import lax
from jax.sharding import PartitionSpec as P

SIDE = 8
ACCUM = 64


def depthwise(images, kernel):
    return lax.conv_general_dilated(
        images,
        kernel[:, :, None, :],
        (1, 1),
        "SAME",
        dimension_numbers=("NHWC", "HWIO", "NHWC"),
        feature_group_count=images.shape[3],
        precision=lax.Precision.HIGHEST,
    )


def gelu_parts(hidden_in):
    cumulative = 0.5 * (1.0 + lax.erf(hidden_in * 0.7071067811865476))
    density = jnp.exp(-0.5 * hidden_in * hidden_in) * 0.3989422804014327
    return (hidden_in * cumulative, cumulative + hidden_in * density)


SWAP = [(0, 1), (1, 0)]


def body(
    tile_rows,
    grad_seq,
    visual_pos,
    assign,
    tile_count,
    kernel,
    norm_gain,
    layer_scale,
    weight_in,
    weight_out,
):
    groups = lax.axis_size("dp")
    height = lax.axis_size("fy")
    width = lax.axis_size("fx")
    shards = height * width
    row_count = tile_rows.shape[0]
    channels = tile_rows.shape[1]
    block_rows = row_count // groups
    half_width = channels // lax.axis_size("llm")
    core_index = lax.axis_index("llm")

    visual = jnp.take(grad_seq, visual_pos[0], axis=0)
    outgoing = jnp.take(visual.reshape(groups, block_rows, channels), assign[0], axis=0).reshape(
        row_count, channels
    )
    out_half = lax.dynamic_slice_in_dim(outgoing, core_index * half_width, half_width, 1)
    arrived_half = lax.all_to_all(out_half, "dp", split_axis=0, concat_axis=0, tiled=True)
    present = jnp.arange(row_count) // (SIDE * SIDE) < tile_count[0]
    mine_half = jnp.where(present[:, None], arrived_half, jnp.zeros_like(arrived_half))
    other_half = lax.ppermute(mine_half, "llm", SWAP)
    first = jnp.where(core_index == 0, mine_half, other_half)
    second = jnp.where(core_index == 0, other_half, mine_half)
    grad_out = jnp.concatenate([first, second], axis=1)

    hid = weight_in.shape[1]
    both = jnp.concatenate([weight_in, weight_out], axis=1)
    y_block = lax.all_gather(both, "fy", axis=0)
    x_tiled = jnp.broadcast_to(y_block[:, None], (height, width) + both.shape)
    both_full = lax.all_to_all(x_tiled, "fx", split_axis=1, concat_axis=1, tiled=True).reshape(
        shards * both.shape[0], both.shape[1]
    )
    w_in_full = both_full[:, :hid]
    w_out_full = both_full[:, hid:]

    mixed = depthwise(
        tile_rows.astype(jnp.float32).reshape(-1, SIDE, SIDE, channels), kernel
    ).reshape(row_count, channels)
    row_mean = jnp.mean(mixed, axis=1, keepdims=True)
    centred = mixed - row_mean
    inv_std = lax.rsqrt(jnp.mean(centred * centred, axis=1, keepdims=True) + 1e-06)
    unit = centred * inv_std
    normed = (unit * norm_gain).astype(jnp.bfloat16)
    hidden_in = jnp.dot(normed, w_in_full, preferred_element_type=jnp.float32)
    activated, slope = gelu_parts(hidden_in)
    hidden = activated.astype(jnp.bfloat16)
    scaled = (grad_out.astype(jnp.float32) * layer_scale).astype(jnp.bfloat16)
    grad_hidden = jnp.dot(scaled, w_out_full, preferred_element_type=jnp.float32)
    grad_pre = (grad_hidden * slope).astype(jnp.bfloat16)

    term_in = lax.dot_general(
        normed, grad_pre, (((0,), (0,)), ((), ())), preferred_element_type=jnp.float32
    )
    term_out = lax.dot_general(
        scaled, hidden, (((0,), (0,)), ((), ())), preferred_element_type=jnp.float32
    )
    terms = jnp.concatenate([term_in, term_out], axis=1).astype(jnp.bfloat16)
    terms = terms.reshape(height, width, channels // shards, 2 * hid)
    x_parts = lax.all_to_all(terms, "fx", split_axis=1, concat_axis=1, tiled=True)
    x_sums = jnp.sum(x_parts.astype(jnp.float32), axis=1).astype(jnp.bfloat16)
    y_parts = lax.all_to_all(x_sums, "fy", split_axis=0, concat_axis=0, tiled=True)
    totals = jnp.sum(y_parts.astype(jnp.float32), axis=0)
    grad_in = totals[:, :hid] / ACCUM
    grad_outw = totals[:, hid:] / ACCUM

    grad_part = lax.dot_general(
        grad_pre, w_in_full, (((1,), (1,)), ((), ())), preferred_element_type=jnp.float32
    )
    part_lo = grad_part[:, :half_width]
    part_hi = grad_part[:, half_width:]
    keep = jnp.where(core_index == 0, part_lo, part_hi)
    send = jnp.where(core_index == 0, part_hi, part_lo).astype(jnp.bfloat16)
    received = lax.ppermute(send, "llm", SWAP)
    grad_normed = keep + received.astype(jnp.float32)
    gain_half = lax.dynamic_slice_in_dim(norm_gain, core_index * half_width, half_width, 0)
    unit_half = lax.dynamic_slice_in_dim(unit, core_index * half_width, half_width, 1)
    grad_unit = grad_normed * gain_half
    sums = jnp.stack(
        [jnp.sum(grad_unit, axis=1), jnp.sum(grad_unit * unit_half, axis=1)], axis=1
    )
    sums = sums + lax.ppermute(sums, "llm", SWAP)
    mean_grad = sums[:, 0:1] / channels
    mean_cross = sums[:, 1:2] / channels
    grad_mixed = inv_std * (grad_unit - mean_grad - unit_half * mean_cross)
    kernel_half = lax.dynamic_slice_in_dim(kernel, core_index * half_width, half_width, 2)
    backward_half = depthwise(
        grad_mixed.reshape(-1, SIDE, SIDE, half_width), kernel_half[::-1, ::-1]
    ).reshape(row_count, half_width)
    grad_tiles = (mine_half.astype(jnp.float32) + backward_half).astype(jnp.bfloat16)
    return (grad_tiles, grad_in, grad_outw)


def x_width(mesh):
    group = mesh.devices[0, :, 0]
    try:
        return len({d.coords[0] for d in group})
    except (AttributeError, TypeError, IndexError):
        return 4


def solution(mesh):
    dp, fsdp, llm = mesh.devices.shape
    width = x_width(mesh)
    split = jax.sharding.Mesh(
        mesh.devices.reshape(dp, fsdp // width, width, llm), ("dp", "fy", "fx", "llm")
    )
    rows = ("dp", "fy", "fx")
    in_specs = (
        P(rows, None),
        P(rows, None),
        P(rows, None),
        P(rows, None),
        P(rows),
        P(),
        P(),
        P(),
        P(("fy", "fx"), "llm"),
        P(("fy", "fx"), "llm"),
    )
    out_specs = (P(rows, "llm"), P(rows, "llm"), P(rows, "llm"))
    return jax.shard_map(body, mesh=split, in_specs=in_specs, out_specs=out_specs, check_vma=False)
```

```python
import jax
import jax.numpy as jnp
from jax import lax
from jax.sharding import PartitionSpec as P

SIDE = 8
ACCUM = 64


def depthwise(images, kernel):
    return lax.conv_general_dilated(
        images,
        kernel[:, :, None, :],
        (1, 1),
        "SAME",
        dimension_numbers=("NHWC", "HWIO", "NHWC"),
        feature_group_count=images.shape[3],
        precision=lax.Precision.HIGHEST,
    )


def gelu_parts(hidden_in):
    cumulative = 0.5 * (1.0 + lax.erf(hidden_in * 0.7071067811865476))
    density = jnp.exp(-0.5 * hidden_in * hidden_in) * 0.3989422804014327
    return (hidden_in * cumulative, cumulative + hidden_in * density)


def to_xy(values, height, width):
    lead = values.shape[:-1]
    grid = values.reshape(lead + (height, width, -1))
    return jnp.swapaxes(grid, -3, -2).reshape(lead + (values.shape[-1],))


SWAP = [(0, 1), (1, 0)]


def body(
    tile_rows,
    grad_seq,
    visual_pos,
    assign,
    tile_count,
    kernel,
    norm_gain,
    layer_scale,
    weight_in,
    weight_out,
):
    groups = lax.axis_size("dp")
    height = lax.axis_size("fy")
    width = lax.axis_size("fx")
    shards = height * width
    row_count = tile_rows.shape[0]
    channels = tile_rows.shape[1]
    block_rows = row_count // groups
    half_width = channels // lax.axis_size("llm")
    core_index = lax.axis_index("llm")

    source_rows = jnp.take(
        visual_pos[0].reshape(groups, block_rows), assign[0], axis=0, mode="clip"
    ).reshape(row_count)
    seq_half = lax.dynamic_slice_in_dim(grad_seq, core_index * half_width, half_width, 1)
    out_half = jnp.take(seq_half, source_rows, axis=0, mode="clip")
    arrived_half = lax.all_to_all(out_half, "dp", split_axis=0, concat_axis=0, tiled=True)
    present = jnp.arange(row_count) // (SIDE * SIDE) < tile_count[0]
    mine_half = jnp.where(present[:, None], arrived_half, jnp.zeros_like(arrived_half))
    other_half = lax.ppermute(mine_half, "llm", SWAP)
    first = jnp.where(core_index == 0, mine_half, other_half)
    second = jnp.where(core_index == 0, other_half, mine_half)
    grad_out = jnp.concatenate([first, second], axis=1)

    hid = weight_in.shape[1]
    both = jnp.concatenate([weight_in, weight_out], axis=1)
    y_block = lax.all_gather(both, "fy", axis=0)
    x_tiled = jnp.broadcast_to(y_block[None], (width,) + y_block.shape)
    both_full = lax.all_to_all(x_tiled, "fx", split_axis=0, concat_axis=0, tiled=True).reshape(
        shards * both.shape[0], both.shape[1]
    )
    w_in_full = both_full[:, :hid]
    w_out_full = both_full[:, hid:]

    mixed = depthwise(
        tile_rows.astype(jnp.float32).reshape(-1, SIDE, SIDE, channels), kernel
    ).reshape(row_count, channels)
    row_mean = jnp.mean(mixed, axis=1, keepdims=True)
    centred = mixed - row_mean
    inv_std = lax.rsqrt(jnp.mean(centred * centred, axis=1, keepdims=True) + 1e-06)
    unit = centred * inv_std
    normed = (unit * norm_gain).astype(jnp.bfloat16)
    normed = to_xy(normed, height, width)
    hidden_in = jnp.dot(normed, w_in_full, preferred_element_type=jnp.float32)
    activated, slope = gelu_parts(hidden_in)
    hidden = activated.astype(jnp.bfloat16)
    scaled = (grad_out.astype(jnp.float32) * layer_scale).astype(jnp.bfloat16)
    scaled = to_xy(scaled, height, width)
    grad_hidden = jnp.dot(scaled, w_out_full, preferred_element_type=jnp.float32)
    grad_pre = (grad_hidden * slope).astype(jnp.bfloat16)

    term_in = lax.dot_general(
        normed, grad_pre, (((0,), (0,)), ((), ())), preferred_element_type=jnp.float32
    )
    term_out = lax.dot_general(
        scaled, hidden, (((0,), (0,)), ((), ())), preferred_element_type=jnp.float32
    )
    terms = jnp.concatenate([term_in, term_out], axis=1).astype(jnp.bfloat16)
    terms = terms.reshape(width, height, channels // shards, 2 * hid)
    x_parts = lax.all_to_all(terms, "fx", split_axis=0, concat_axis=0, tiled=True)
    x_sums = jnp.sum(x_parts.astype(jnp.float32), axis=0).astype(jnp.bfloat16)
    y_parts = lax.all_to_all(x_sums, "fy", split_axis=0, concat_axis=0, tiled=True)
    totals = jnp.sum(y_parts.astype(jnp.float32), axis=0)
    grad_in = totals[:, :hid] / ACCUM
    grad_outw = totals[:, hid:] / ACCUM

    grad_part = lax.dot_general(
        grad_pre, w_in_full, (((1,), (1,)), ((), ())), preferred_element_type=jnp.float32
    )
    grad_part = to_xy(grad_part, width, height)
    part_lo = grad_part[:, :half_width]
    part_hi = grad_part[:, half_width:]
    keep = jnp.where(core_index == 0, part_lo, part_hi)
    send = jnp.where(core_index == 0, part_hi, part_lo).astype(jnp.bfloat16)
    received = lax.ppermute(send, "llm", SWAP)
    grad_normed = keep + received.astype(jnp.float32)
    gain_half = lax.dynamic_slice_in_dim(norm_gain, core_index * half_width, half_width, 0)
    unit_half = lax.dynamic_slice_in_dim(unit, core_index * half_width, half_width, 1)
    grad_unit = grad_normed * gain_half
    sums = jnp.stack(
        [jnp.sum(grad_unit, axis=1), jnp.sum(grad_unit * unit_half, axis=1)], axis=1
    )
    sums = sums + lax.ppermute(sums, "llm", SWAP)
    mean_grad = sums[:, 0:1] / channels
    mean_cross = sums[:, 1:2] / channels
    grad_mixed = inv_std * (grad_unit - mean_grad - unit_half * mean_cross)
    kernel_half = lax.dynamic_slice_in_dim(kernel, core_index * half_width, half_width, 2)
    backward_half = depthwise(
        grad_mixed.reshape(-1, SIDE, SIDE, half_width), kernel_half[::-1, ::-1]
    ).reshape(row_count, half_width)
    grad_tiles = (mine_half.astype(jnp.float32) + backward_half).astype(jnp.bfloat16)
    return (grad_tiles, grad_in, grad_outw)


def x_width(mesh):
    group = mesh.devices[0, :, 0]
    try:
        return len({d.coords[0] for d in group})
    except (AttributeError, TypeError, IndexError):
        return 4


def solution(mesh):
    dp, fsdp, llm = mesh.devices.shape
    width = x_width(mesh)
    split = jax.sharding.Mesh(
        mesh.devices.reshape(dp, fsdp // width, width, llm), ("dp", "fy", "fx", "llm")
    )
    rows = ("dp", "fy", "fx")
    in_specs = (
        P(rows, None),
        P(rows, None),
        P(rows, None),
        P(rows, None),
        P(rows),
        P(),
        P(),
        P(),
        P(("fy", "fx"), "llm"),
        P(("fy", "fx"), "llm"),
    )
    out_specs = (P(rows, "llm"), P(rows, "llm"), P(rows, "llm"))
    return jax.shard_map(body, mesh=split, in_specs=in_specs, out_specs=out_specs, check_vma=False)
```

```python
import jax
import jax.numpy as jnp
from jax import lax
from jax.sharding import PartitionSpec as P

SIDE = 8
ACCUM = 64


def depthwise(images, kernel):
    return lax.conv_general_dilated(
        images,
        kernel[:, :, None, :],
        (1, 1),
        "SAME",
        dimension_numbers=("NHWC", "HWIO", "NHWC"),
        feature_group_count=images.shape[3],
        precision=lax.Precision.HIGHEST,
    )


def gelu_parts(hidden_in):
    cumulative = 0.5 * (1.0 + lax.erf(hidden_in * 0.7071067811865476))
    density = jnp.exp(-0.5 * hidden_in * hidden_in) * 0.3989422804014327
    return (hidden_in * cumulative, cumulative + hidden_in * density)


SWAP = [(0, 1), (1, 0)]


def body(
    tile_rows,
    grad_seq,
    visual_pos,
    assign,
    tile_count,
    kernel,
    norm_gain,
    layer_scale,
    weight_in,
    weight_out,
):
    groups = lax.axis_size("dp")
    height = lax.axis_size("fy")
    width = lax.axis_size("fx")
    shards = height * width
    row_count = tile_rows.shape[0]
    channels = tile_rows.shape[1]
    block_rows = row_count // groups
    half_width = channels // lax.axis_size("llm")
    core_index = lax.axis_index("llm")

    source_rows = jnp.take(
        visual_pos[0].reshape(groups, block_rows), assign[0], axis=0, mode="clip"
    ).reshape(row_count)
    seq_half = lax.dynamic_slice_in_dim(grad_seq, core_index * half_width, half_width, 1)
    out_half = jnp.take(seq_half, source_rows, axis=0, mode="clip")
    arrived_half = lax.all_to_all(out_half, "dp", split_axis=0, concat_axis=0, tiled=True)
    present = jnp.arange(row_count) // (SIDE * SIDE) < tile_count[0]
    mine_half = jnp.where(present[:, None], arrived_half, jnp.zeros_like(arrived_half))
    other_half = lax.ppermute(mine_half, "llm", SWAP)
    first = jnp.where(core_index == 0, mine_half, other_half)
    second = jnp.where(core_index == 0, other_half, mine_half)
    grad_out = jnp.concatenate([first, second], axis=1)

    hid = weight_in.shape[1]
    both = jnp.concatenate([weight_in, weight_out], axis=1)
    y_block = lax.all_gather(both, "fy", axis=0)
    x_tiled = jnp.broadcast_to(y_block[:, None], (height, width) + both.shape)
    both_full = lax.all_to_all(x_tiled, "fx", split_axis=1, concat_axis=1, tiled=True).reshape(
        shards * both.shape[0], both.shape[1]
    )
    w_in_full = both_full[:, :hid]
    w_out_full = both_full[:, hid:]

    mixed = depthwise(
        tile_rows.astype(jnp.float32).reshape(-1, SIDE, SIDE, channels), kernel
    ).reshape(row_count, channels)
    row_mean = jnp.mean(mixed, axis=1, keepdims=True)
    centred = mixed - row_mean
    inv_std = lax.rsqrt(jnp.mean(centred * centred, axis=1, keepdims=True) + 1e-06)
    unit = centred * inv_std
    normed = (unit * norm_gain).astype(jnp.bfloat16)
    hidden_in = jnp.dot(normed, w_in_full, preferred_element_type=jnp.float32)
    activated, slope = gelu_parts(hidden_in)
    hidden = activated.astype(jnp.bfloat16)
    scaled = (grad_out.astype(jnp.float32) * layer_scale).astype(jnp.bfloat16)
    grad_hidden = jnp.dot(scaled, w_out_full, preferred_element_type=jnp.float32)
    grad_pre = (grad_hidden * slope).astype(jnp.bfloat16)

    term_in = lax.dot_general(
        normed, grad_pre, (((0,), (0,)), ((), ())), preferred_element_type=jnp.float32
    )
    term_out = lax.dot_general(
        scaled, hidden, (((0,), (0,)), ((), ())), preferred_element_type=jnp.float32
    )
    terms = jnp.concatenate([term_in, term_out], axis=1).astype(jnp.bfloat16)
    terms = terms.reshape(height, width, channels // shards, 2 * hid)
    x_parts = lax.all_to_all(terms, "fx", split_axis=1, concat_axis=1, tiled=True)
    x_sums = jnp.sum(x_parts.astype(jnp.float32), axis=1).astype(jnp.bfloat16)
    y_parts = lax.all_to_all(x_sums, "fy", split_axis=0, concat_axis=0, tiled=True)
    totals = jnp.sum(y_parts.astype(jnp.float32), axis=0)
    grad_in = totals[:, :hid] / ACCUM
    grad_outw = totals[:, hid:] / ACCUM

    grad_part = lax.dot_general(
        grad_pre, w_in_full, (((1,), (1,)), ((), ())), preferred_element_type=jnp.float32
    )
    part_lo = grad_part[:, :half_width]
    part_hi = grad_part[:, half_width:]
    keep = jnp.where(core_index == 0, part_lo, part_hi)
    send = jnp.where(core_index == 0, part_hi, part_lo).astype(jnp.bfloat16)
    received = lax.ppermute(send, "llm", SWAP)
    grad_normed = keep + received.astype(jnp.float32)
    gain_half = lax.dynamic_slice_in_dim(norm_gain, core_index * half_width, half_width, 0)
    unit_half = lax.dynamic_slice_in_dim(unit, core_index * half_width, half_width, 1)
    grad_unit = grad_normed * gain_half
    sums = jnp.stack(
        [jnp.sum(grad_unit, axis=1), jnp.sum(grad_unit * unit_half, axis=1)], axis=1
    )
    sums = sums + lax.ppermute(sums, "llm", SWAP)
    mean_grad = sums[:, 0:1] / channels
    mean_cross = sums[:, 1:2] / channels
    grad_mixed = inv_std * (grad_unit - mean_grad - unit_half * mean_cross)
    kernel_half = lax.dynamic_slice_in_dim(kernel, core_index * half_width, half_width, 2)
    backward_half = depthwise(
        grad_mixed.reshape(-1, SIDE, SIDE, half_width), kernel_half[::-1, ::-1]
    ).reshape(row_count, half_width)
    grad_tiles = (mine_half.astype(jnp.float32) + backward_half).astype(jnp.bfloat16)
    return (grad_tiles, grad_in, grad_outw)


def x_width(mesh):
    group = mesh.devices[0, :, 0]
    try:
        return len({d.coords[0] for d in group})
    except (AttributeError, TypeError, IndexError):
        return 4


def solution(mesh):
    dp, fsdp, llm = mesh.devices.shape
    width = x_width(mesh)
    split = jax.sharding.Mesh(
        mesh.devices.reshape(dp, fsdp // width, width, llm), ("dp", "fy", "fx", "llm")
    )
    rows = ("dp", "fy", "fx")
    in_specs = (
        P(rows, None),
        P(rows, None),
        P(rows, None),
        P(rows, None),
        P(rows),
        P(),
        P(),
        P(),
        P(("fy", "fx"), "llm"),
        P(("fy", "fx"), "llm"),
    )
    out_specs = (P(rows, "llm"), P(rows, "llm"), P(rows, "llm"))
    return jax.shard_map(body, mesh=split, in_specs=in_specs, out_specs=out_specs, check_vma=False)
```

```python
import jax
import jax.numpy as jnp
from jax import lax
from jax.sharding import PartitionSpec as P

SIDE = 8
ACCUM = 64


def depthwise(images, kernel):
    return lax.conv_general_dilated(
        images,
        kernel[:, :, None, :],
        (1, 1),
        "SAME",
        dimension_numbers=("NHWC", "HWIO", "NHWC"),
        feature_group_count=images.shape[3],
        precision=lax.Precision.HIGHEST,
    )


def gelu_parts(hidden_in):
    cumulative = 0.5 * (1.0 + lax.erf(hidden_in * 0.7071067811865476))
    density = jnp.exp(-0.5 * hidden_in * hidden_in) * 0.3989422804014327
    return (hidden_in * cumulative, cumulative + hidden_in * density)


SWAP = [(0, 1), (1, 0)]


def body(
    tile_rows,
    grad_seq,
    visual_pos,
    assign,
    tile_count,
    kernel,
    norm_gain,
    layer_scale,
    weight_in,
    weight_out,
):
    groups = lax.axis_size("dp")
    height = lax.axis_size("fyh") * lax.axis_size("fyl")
    width = lax.axis_size("fx")
    shards = height * width
    row_count = tile_rows.shape[0]
    channels = tile_rows.shape[1]
    block_rows = row_count // groups
    half_width = channels // lax.axis_size("llm")
    core_index = lax.axis_index("llm")

    source_rows = jnp.take(
        visual_pos[0].reshape(groups, block_rows), assign[0], axis=0, mode="clip"
    ).reshape(row_count)
    seq_half = lax.dynamic_slice_in_dim(grad_seq, core_index * half_width, half_width, 1)
    out_half = jnp.take(seq_half, source_rows, axis=0, mode="clip")
    arrived_half = lax.all_to_all(out_half, "dp", split_axis=0, concat_axis=0, tiled=True)
    present = jnp.arange(row_count) // (SIDE * SIDE) < tile_count[0]
    mine_half = jnp.where(present[:, None], arrived_half, jnp.zeros_like(arrived_half))
    other_half = lax.ppermute(mine_half, "llm", SWAP)
    first = jnp.where(core_index == 0, mine_half, other_half)
    second = jnp.where(core_index == 0, other_half, mine_half)
    grad_out = jnp.concatenate([first, second], axis=1)

    hid = weight_in.shape[1]
    both = jnp.concatenate([weight_in, weight_out], axis=1)
    y_low = lax.all_gather(both, "fyl", axis=0)
    y_block = lax.all_gather(y_low, "fyh", axis=0).reshape((height,) + both.shape)
    x_tiled = jnp.broadcast_to(y_block[:, None], (height, width) + both.shape)
    both_full = lax.all_to_all(x_tiled, "fx", split_axis=1, concat_axis=1, tiled=True).reshape(
        shards * both.shape[0], both.shape[1]
    )
    w_in_full = both_full[:, :hid]
    w_out_full = both_full[:, hid:]

    mixed = depthwise(
        tile_rows.astype(jnp.float32).reshape(-1, SIDE, SIDE, channels), kernel
    ).reshape(row_count, channels)
    row_mean = jnp.mean(mixed, axis=1, keepdims=True)
    centred = mixed - row_mean
    inv_std = lax.rsqrt(jnp.mean(centred * centred, axis=1, keepdims=True) + 1e-06)
    unit = centred * inv_std
    normed = (unit * norm_gain).astype(jnp.bfloat16)
    hidden_in = jnp.dot(normed, w_in_full, preferred_element_type=jnp.float32)
    activated, slope = gelu_parts(hidden_in)
    hidden = activated.astype(jnp.bfloat16)
    scaled = (grad_out.astype(jnp.float32) * layer_scale).astype(jnp.bfloat16)
    grad_hidden = jnp.dot(scaled, w_out_full, preferred_element_type=jnp.float32)
    grad_pre = (grad_hidden * slope).astype(jnp.bfloat16)

    term_in = lax.dot_general(
        normed, grad_pre, (((0,), (0,)), ((), ())), preferred_element_type=jnp.float32
    )
    term_out = lax.dot_general(
        scaled, hidden, (((0,), (0,)), ((), ())), preferred_element_type=jnp.float32
    )
    terms = jnp.concatenate([term_in, term_out], axis=1).astype(jnp.bfloat16)
    terms = terms.reshape(height, width, channels // shards, 2 * hid)
    x_parts = lax.all_to_all(terms, "fx", split_axis=1, concat_axis=1, tiled=True)
    x_sums = jnp.sum(x_parts.astype(jnp.float32), axis=1).astype(jnp.bfloat16)
    y_parts = lax.all_to_all(x_sums, ("fyh", "fyl"), split_axis=0, concat_axis=0, tiled=True)
    totals = jnp.sum(y_parts.astype(jnp.float32), axis=0)
    grad_in = totals[:, :hid] / ACCUM
    grad_outw = totals[:, hid:] / ACCUM

    grad_part = lax.dot_general(
        grad_pre, w_in_full, (((1,), (1,)), ((), ())), preferred_element_type=jnp.float32
    )
    part_lo = grad_part[:, :half_width]
    part_hi = grad_part[:, half_width:]
    keep = jnp.where(core_index == 0, part_lo, part_hi)
    send = jnp.where(core_index == 0, part_hi, part_lo).astype(jnp.bfloat16)
    received = lax.ppermute(send, "llm", SWAP)
    grad_normed = keep + received.astype(jnp.float32)
    gain_half = lax.dynamic_slice_in_dim(norm_gain, core_index * half_width, half_width, 0)
    unit_half = lax.dynamic_slice_in_dim(unit, core_index * half_width, half_width, 1)
    grad_unit = grad_normed * gain_half
    sums = jnp.stack(
        [jnp.sum(grad_unit, axis=1), jnp.sum(grad_unit * unit_half, axis=1)], axis=1
    )
    sums = sums + lax.ppermute(sums, "llm", SWAP)
    mean_grad = sums[:, 0:1] / channels
    mean_cross = sums[:, 1:2] / channels
    grad_mixed = inv_std * (grad_unit - mean_grad - unit_half * mean_cross)
    kernel_half = lax.dynamic_slice_in_dim(kernel, core_index * half_width, half_width, 2)
    backward_half = depthwise(
        grad_mixed.reshape(-1, SIDE, SIDE, half_width), kernel_half[::-1, ::-1]
    ).reshape(row_count, half_width)
    grad_tiles = (mine_half.astype(jnp.float32) + backward_half).astype(jnp.bfloat16)
    return (grad_tiles, grad_in, grad_outw)


def x_width(mesh):
    group = mesh.devices[0, :, 0]
    try:
        return len({d.coords[0] for d in group})
    except (AttributeError, TypeError, IndexError):
        return 4


def solution(mesh):
    dp, fsdp, llm = mesh.devices.shape
    width = x_width(mesh)
    height = fsdp // width
    low = height // 2 if height % 2 == 0 else height
    split = jax.sharding.Mesh(
        mesh.devices.reshape(dp, height // low, low, width, llm),
        ("dp", "fyh", "fyl", "fx", "llm"),
    )
    rows = ("dp", "fyh", "fyl", "fx")
    in_specs = (
        P(rows, None),
        P(rows, None),
        P(rows, None),
        P(rows, None),
        P(rows),
        P(),
        P(),
        P(),
        P(("fyh", "fyl", "fx"), "llm"),
        P(("fyh", "fyl", "fx"), "llm"),
    )
    out_specs = (P(rows, "llm"), P(rows, "llm"), P(rows, "llm"))
    return jax.shard_map(body, mesh=split, in_specs=in_specs, out_specs=out_specs, check_vma=False)
```

```python
import jax
import jax.numpy as jnp
from jax import lax
from jax.sharding import PartitionSpec as P

SIDE = 8
ACCUM = 64


def depthwise(images, kernel):
    return lax.conv_general_dilated(
        images,
        kernel[:, :, None, :],
        (1, 1),
        "SAME",
        dimension_numbers=("NHWC", "HWIO", "NHWC"),
        feature_group_count=images.shape[3],
        precision=lax.Precision.HIGHEST,
    )


def gelu_parts(hidden_in):
    cumulative = 0.5 * (1.0 + lax.erf(hidden_in * 0.7071067811865476))
    density = jnp.exp(-0.5 * hidden_in * hidden_in) * 0.3989422804014327
    return (hidden_in * cumulative, cumulative + hidden_in * density)


SWAP = [(0, 1), (1, 0)]


def body(
    tile_rows,
    grad_seq,
    visual_pos,
    assign,
    tile_count,
    kernel,
    norm_gain,
    layer_scale,
    weight_in,
    weight_out,
):
    groups = lax.axis_size("dp")
    height = lax.axis_size("fy")
    width = lax.axis_size("fx")
    shards = height * width
    row_count = tile_rows.shape[0]
    channels = tile_rows.shape[1]
    block_rows = row_count // groups
    half_width = channels // lax.axis_size("llm")
    core_index = lax.axis_index("llm")

    flat = (assign[0][:, None] * block_rows + jnp.arange(block_rows)[None, :]).reshape(row_count)
    source_rows = jnp.take(visual_pos, flat, axis=1, mode="clip")[0]
    seq_half = lax.dynamic_slice_in_dim(grad_seq, core_index * half_width, half_width, 1)
    pick = source_rows[:, None] == jnp.arange(grad_seq.shape[0])[None, :]
    out_half = jnp.dot(
        pick.astype(seq_half.dtype), seq_half, preferred_element_type=jnp.float32
    ).astype(seq_half.dtype)
    arrived_half = lax.all_to_all(out_half, "dp", split_axis=0, concat_axis=0, tiled=True)
    present = jnp.arange(row_count) // (SIDE * SIDE) < tile_count[0]
    mine_half = jnp.where(present[:, None], arrived_half, jnp.zeros_like(arrived_half))
    other_half = lax.ppermute(mine_half, "llm", SWAP)
    first = jnp.where(core_index == 0, mine_half, other_half)
    second = jnp.where(core_index == 0, other_half, mine_half)
    grad_out = jnp.concatenate([first, second], axis=1)

    hid = weight_in.shape[1]
    both = jnp.concatenate([weight_in, weight_out], axis=1)
    y_block = lax.all_gather(both, "fy", axis=0)
    x_tiled = jnp.broadcast_to(y_block[:, None], (height, width) + both.shape)
    both_full = lax.all_to_all(x_tiled, "fx", split_axis=1, concat_axis=1, tiled=True).reshape(
        shards * both.shape[0], both.shape[1]
    )
    w_in_full = both_full[:, :hid]
    w_out_full = both_full[:, hid:]

    mixed = depthwise(
        tile_rows.astype(jnp.float32).reshape(-1, SIDE, SIDE, channels), kernel
    ).reshape(row_count, channels)
    row_mean = jnp.mean(mixed, axis=1, keepdims=True)
    centred = mixed - row_mean
    inv_std = lax.rsqrt(jnp.mean(centred * centred, axis=1, keepdims=True) + 1e-06)
    unit = centred * inv_std
    normed = (unit * norm_gain).astype(jnp.bfloat16)
    hidden_in = jnp.dot(normed, w_in_full, preferred_element_type=jnp.float32)
    activated, slope = gelu_parts(hidden_in)
    hidden = activated.astype(jnp.bfloat16)
    scaled = (grad_out.astype(jnp.float32) * layer_scale).astype(jnp.bfloat16)
    grad_hidden = jnp.dot(scaled, w_out_full, preferred_element_type=jnp.float32)
    grad_pre = (grad_hidden * slope).astype(jnp.bfloat16)

    term_in = lax.dot_general(
        normed, grad_pre, (((0,), (0,)), ((), ())), preferred_element_type=jnp.float32
    )
    term_out = lax.dot_general(
        scaled, hidden, (((0,), (0,)), ((), ())), preferred_element_type=jnp.float32
    )
    terms = jnp.concatenate([term_in, term_out], axis=1).astype(jnp.bfloat16)
    terms = terms.reshape(height, width, channels // shards, 2 * hid)
    x_parts = lax.all_to_all(terms, "fx", split_axis=1, concat_axis=1, tiled=True)
    x_sums = jnp.sum(x_parts.astype(jnp.float32), axis=1).astype(jnp.bfloat16)
    y_parts = lax.all_to_all(x_sums, "fy", split_axis=0, concat_axis=0, tiled=True)
    totals = jnp.sum(y_parts.astype(jnp.float32), axis=0)
    grad_in = totals[:, :hid] / ACCUM
    grad_outw = totals[:, hid:] / ACCUM

    grad_part = lax.dot_general(
        grad_pre, w_in_full, (((1,), (1,)), ((), ())), preferred_element_type=jnp.float32
    )
    part_lo = grad_part[:, :half_width]
    part_hi = grad_part[:, half_width:]
    keep = jnp.where(core_index == 0, part_lo, part_hi)
    send = jnp.where(core_index == 0, part_hi, part_lo).astype(jnp.bfloat16)
    received = lax.ppermute(send, "llm", SWAP)
    grad_normed = keep + received.astype(jnp.float32)
    gain_half = lax.dynamic_slice_in_dim(norm_gain, core_index * half_width, half_width, 0)
    unit_half = lax.dynamic_slice_in_dim(unit, core_index * half_width, half_width, 1)
    grad_unit = grad_normed * gain_half
    sums = jnp.stack(
        [jnp.sum(grad_unit, axis=1), jnp.sum(grad_unit * unit_half, axis=1)], axis=1
    )
    sums = sums + lax.ppermute(sums, "llm", SWAP)
    mean_grad = sums[:, 0:1] / channels
    mean_cross = sums[:, 1:2] / channels
    grad_mixed = inv_std * (grad_unit - mean_grad - unit_half * mean_cross)
    kernel_half = lax.dynamic_slice_in_dim(kernel, core_index * half_width, half_width, 2)
    backward_half = depthwise(
        grad_mixed.reshape(-1, SIDE, SIDE, half_width), kernel_half[::-1, ::-1]
    ).reshape(row_count, half_width)
    grad_tiles = (mine_half.astype(jnp.float32) + backward_half).astype(jnp.bfloat16)
    return (grad_tiles, grad_in, grad_outw)


def x_width(mesh):
    group = mesh.devices[0, :, 0]
    try:
        return len({d.coords[0] for d in group})
    except (AttributeError, TypeError, IndexError):
        return 4


def solution(mesh):
    dp, fsdp, llm = mesh.devices.shape
    width = x_width(mesh)
    split = jax.sharding.Mesh(
        mesh.devices.reshape(dp, fsdp // width, width, llm), ("dp", "fy", "fx", "llm")
    )
    rows = ("dp", "fy", "fx")
    in_specs = (
        P(rows, None),
        P(rows, None),
        P(rows, None),
        P(rows, None),
        P(rows),
        P(),
        P(),
        P(),
        P(("fy", "fx"), "llm"),
        P(("fy", "fx"), "llm"),
    )
    out_specs = (P(rows, "llm"), P(rows, "llm"), P(rows, "llm"))
    return jax.shard_map(body, mesh=split, in_specs=in_specs, out_specs=out_specs, check_vma=False)
```

```python
import jax
import jax.numpy as jnp
from jax import lax
from jax.sharding import PartitionSpec as P

SIDE = 8
ACCUM = 64


def depthwise(images, kernel):
    return lax.conv_general_dilated(
        images,
        kernel[:, :, None, :],
        (1, 1),
        "SAME",
        dimension_numbers=("NHWC", "HWIO", "NHWC"),
        feature_group_count=images.shape[3],
        precision=lax.Precision.HIGHEST,
    )


def gelu_parts(hidden_in):
    cumulative = 0.5 * (1.0 + lax.erf(hidden_in * 0.7071067811865476))
    density = jnp.exp(-0.5 * hidden_in * hidden_in) * 0.3989422804014327
    return (hidden_in * cumulative, cumulative + hidden_in * density)


def rows_xy(values, height, width):
    grid = values.reshape((height, width, -1) + values.shape[1:])
    return jnp.swapaxes(grid, 0, 1).reshape(values.shape)


SWAP = [(0, 1), (1, 0)]


def body(
    tile_rows,
    grad_seq,
    visual_pos,
    assign,
    tile_count,
    kernel,
    norm_gain,
    layer_scale,
    weight_in,
    weight_out,
):
    groups = lax.axis_size("dp")
    height = lax.axis_size("fy")
    width = lax.axis_size("fx")
    shards = height * width
    row_count = tile_rows.shape[0]
    channels = tile_rows.shape[1]
    block_rows = row_count // groups
    half_width = channels // lax.axis_size("llm")
    core_index = lax.axis_index("llm")

    flat = (assign[0][:, None] * block_rows + jnp.arange(block_rows)[None, :]).reshape(row_count)
    source_rows = jnp.take(visual_pos, flat, axis=1, mode="clip")[0]
    seq_half = lax.dynamic_slice_in_dim(grad_seq, core_index * half_width, half_width, 1)
    pick = source_rows[:, None] == jnp.arange(grad_seq.shape[0])[None, :]
    out_half = jnp.dot(
        pick.astype(seq_half.dtype), seq_half, preferred_element_type=jnp.float32
    ).astype(seq_half.dtype)
    arrived_half = lax.all_to_all(out_half, "dp", split_axis=0, concat_axis=0, tiled=True)
    present = jnp.arange(row_count) // (SIDE * SIDE) < tile_count[0]
    mine_half = jnp.where(present[:, None], arrived_half, jnp.zeros_like(arrived_half))
    other_half = lax.ppermute(mine_half, "llm", SWAP)
    first = jnp.where(core_index == 0, mine_half, other_half)
    second = jnp.where(core_index == 0, other_half, mine_half)
    grad_out = jnp.concatenate([first, second], axis=1)

    hid = weight_in.shape[1]
    both = jnp.concatenate([weight_in, weight_out], axis=1)
    y_block = lax.all_gather(both, "fy", axis=0)
    x_tiled = jnp.broadcast_to(y_block[:, None], (height, width) + both.shape)
    both_full = lax.all_to_all(x_tiled, "fx", split_axis=1, concat_axis=1, tiled=True).reshape(
        shards * both.shape[0], both.shape[1]
    )
    w_in_full = both_full[:, :hid]
    w_out_full = both_full[:, hid:]

    mixed = depthwise(
        tile_rows.astype(jnp.float32).reshape(-1, SIDE, SIDE, channels), kernel
    ).reshape(row_count, channels)
    row_mean = jnp.mean(mixed, axis=1, keepdims=True)
    centred = mixed - row_mean
    inv_std = lax.rsqrt(jnp.mean(centred * centred, axis=1, keepdims=True) + 1e-06)
    unit = centred * inv_std
    normed = (unit * norm_gain).astype(jnp.bfloat16)
    hidden_in = jnp.dot(normed, w_in_full, preferred_element_type=jnp.float32)
    activated, slope = gelu_parts(hidden_in)
    hidden = activated.astype(jnp.bfloat16)
    scaled = (grad_out.astype(jnp.float32) * layer_scale).astype(jnp.bfloat16)
    grad_hidden = jnp.dot(scaled, w_out_full, preferred_element_type=jnp.float32)
    grad_pre = (grad_hidden * slope).astype(jnp.bfloat16)

    term_in = jnp.dot(
        rows_xy(normed.T, height, width), grad_pre, preferred_element_type=jnp.float32
    )
    term_out = jnp.dot(
        rows_xy(scaled.T, height, width), hidden, preferred_element_type=jnp.float32
    )
    terms = jnp.concatenate([term_in, term_out], axis=1).astype(jnp.bfloat16)
    terms = terms.reshape(width, height, channels // shards, 2 * hid)
    x_parts = lax.all_to_all(terms, "fx", split_axis=0, concat_axis=0, tiled=True)
    x_sums = jnp.sum(x_parts.astype(jnp.float32), axis=0).astype(jnp.bfloat16)
    y_parts = lax.all_to_all(x_sums, "fy", split_axis=0, concat_axis=0, tiled=True)
    totals = jnp.sum(y_parts.astype(jnp.float32), axis=0)
    grad_in = totals[:, :hid] / ACCUM
    grad_outw = totals[:, hid:] / ACCUM

    grad_part = lax.dot_general(
        grad_pre, w_in_full, (((1,), (1,)), ((), ())), preferred_element_type=jnp.float32
    )
    part_lo = grad_part[:, :half_width]
    part_hi = grad_part[:, half_width:]
    keep = jnp.where(core_index == 0, part_lo, part_hi)
    send = jnp.where(core_index == 0, part_hi, part_lo).astype(jnp.bfloat16)
    received = lax.ppermute(send, "llm", SWAP)
    grad_normed = keep + received.astype(jnp.float32)
    gain_half = lax.dynamic_slice_in_dim(norm_gain, core_index * half_width, half_width, 0)
    unit_half = lax.dynamic_slice_in_dim(unit, core_index * half_width, half_width, 1)
    grad_unit = grad_normed * gain_half
    sums = jnp.stack(
        [jnp.sum(grad_unit, axis=1), jnp.sum(grad_unit * unit_half, axis=1)], axis=1
    )
    sums = sums + lax.ppermute(sums, "llm", SWAP)
    mean_grad = sums[:, 0:1] / channels
    mean_cross = sums[:, 1:2] / channels
    grad_mixed = inv_std * (grad_unit - mean_grad - unit_half * mean_cross)
    kernel_half = lax.dynamic_slice_in_dim(kernel, core_index * half_width, half_width, 2)
    backward_half = depthwise(
        grad_mixed.reshape(-1, SIDE, SIDE, half_width), kernel_half[::-1, ::-1]
    ).reshape(row_count, half_width)
    grad_tiles = (mine_half.astype(jnp.float32) + backward_half).astype(jnp.bfloat16)
    return (grad_tiles, grad_in, grad_outw)


def x_width(mesh):
    group = mesh.devices[0, :, 0]
    try:
        return len({d.coords[0] for d in group})
    except (AttributeError, TypeError, IndexError):
        return 4


def solution(mesh):
    dp, fsdp, llm = mesh.devices.shape
    width = x_width(mesh)
    split = jax.sharding.Mesh(
        mesh.devices.reshape(dp, fsdp // width, width, llm), ("dp", "fy", "fx", "llm")
    )
    rows = ("dp", "fy", "fx")
    in_specs = (
        P(rows, None),
        P(rows, None),
        P(rows, None),
        P(rows, None),
        P(rows),
        P(),
        P(),
        P(),
        P(("fy", "fx"), "llm"),
        P(("fy", "fx"), "llm"),
    )
    out_specs = (P(rows, "llm"), P(rows, "llm"), P(rows, "llm"))
    return jax.shard_map(body, mesh=split, in_specs=in_specs, out_specs=out_specs, check_vma=False)
```

```python
import jax
import jax.numpy as jnp
from jax import lax
from jax.sharding import PartitionSpec as P

SIDE = 8
ACCUM = 64


def depthwise(images, kernel):
    return lax.conv_general_dilated(
        images,
        kernel[:, :, None, :],
        (1, 1),
        "SAME",
        dimension_numbers=("NHWC", "HWIO", "NHWC"),
        feature_group_count=images.shape[3],
        precision=lax.Precision.HIGHEST,
    )


def gelu_parts(hidden_in):
    cumulative = 0.5 * (1.0 + lax.erf(hidden_in * 0.7071067811865476))
    density = jnp.exp(-0.5 * hidden_in * hidden_in) * 0.3989422804014327
    return (hidden_in * cumulative, cumulative + hidden_in * density)


SWAP = [(0, 1), (1, 0)]


def body(
    tile_rows,
    grad_seq,
    visual_pos,
    assign,
    tile_count,
    kernel,
    norm_gain,
    layer_scale,
    weight_in,
    weight_out,
):
    groups = lax.axis_size("dp")
    height = lax.axis_size("fy")
    width = lax.axis_size("fx")
    shards = height * width
    row_count = tile_rows.shape[0]
    channels = tile_rows.shape[1]
    block_rows = row_count // groups
    half_width = channels // lax.axis_size("llm")
    core_index = lax.axis_index("llm")

    flat = (assign[0][:, None] * block_rows + jnp.arange(block_rows)[None, :]).reshape(row_count)
    chosen = flat[:, None] == jnp.arange(visual_pos.shape[1])[None, :]
    source_rows = jnp.sum(jnp.where(chosen, visual_pos, 0), axis=1)
    seq_half = lax.dynamic_slice_in_dim(grad_seq, core_index * half_width, half_width, 1)
    pick = source_rows[:, None] == jnp.arange(grad_seq.shape[0])[None, :]
    out_half = jnp.dot(
        pick.astype(seq_half.dtype), seq_half, preferred_element_type=jnp.float32
    ).astype(seq_half.dtype)
    arrived_half = lax.all_to_all(out_half, "dp", split_axis=0, concat_axis=0, tiled=True)
    present = jnp.arange(row_count) // (SIDE * SIDE) < tile_count[0]
    mine_half = jnp.where(present[:, None], arrived_half, jnp.zeros_like(arrived_half))
    other_half = lax.ppermute(mine_half, "llm", SWAP)
    first = jnp.where(core_index == 0, mine_half, other_half)
    second = jnp.where(core_index == 0, other_half, mine_half)
    grad_out = jnp.concatenate([first, second], axis=1)

    hid = weight_in.shape[1]
    both = jnp.concatenate([weight_in, weight_out], axis=1)
    y_block = lax.all_gather(both, "fy", axis=0)
    x_tiled = jnp.broadcast_to(y_block[:, None], (height, width) + both.shape)
    both_full = lax.all_to_all(x_tiled, "fx", split_axis=1, concat_axis=1, tiled=True).reshape(
        shards * both.shape[0], both.shape[1]
    )
    w_in_full = both_full[:, :hid]
    w_out_full = both_full[:, hid:]

    mixed = depthwise(
        tile_rows.astype(jnp.float32).reshape(-1, SIDE, SIDE, channels), kernel
    ).reshape(row_count, channels)
    row_mean = jnp.mean(mixed, axis=1, keepdims=True)
    centred = mixed - row_mean
    inv_std = lax.rsqrt(jnp.mean(centred * centred, axis=1, keepdims=True) + 1e-06)
    unit = centred * inv_std
    normed = (unit * norm_gain).astype(jnp.bfloat16)
    hidden_in = jnp.dot(normed, w_in_full, preferred_element_type=jnp.float32)
    activated, slope = gelu_parts(hidden_in)
    hidden = activated.astype(jnp.bfloat16)
    scaled = (grad_out.astype(jnp.float32) * layer_scale).astype(jnp.bfloat16)
    grad_hidden = jnp.dot(scaled, w_out_full, preferred_element_type=jnp.float32)
    grad_pre = (grad_hidden * slope).astype(jnp.bfloat16)

    term_in = lax.dot_general(
        normed, grad_pre, (((0,), (0,)), ((), ())), preferred_element_type=jnp.float32
    )
    term_out = lax.dot_general(
        scaled, hidden, (((0,), (0,)), ((), ())), preferred_element_type=jnp.float32
    )
    terms = jnp.concatenate([term_in, term_out], axis=1).astype(jnp.bfloat16)
    terms = terms.reshape(height, width, channels // shards, 2 * hid)
    x_parts = lax.all_to_all(terms, "fx", split_axis=1, concat_axis=1, tiled=True)
    x_sums = jnp.sum(x_parts.astype(jnp.float32), axis=1).astype(jnp.bfloat16)
    y_parts = lax.all_to_all(x_sums, "fy", split_axis=0, concat_axis=0, tiled=True)
    totals = jnp.sum(y_parts.astype(jnp.float32), axis=0)
    grad_in = totals[:, :hid] / ACCUM
    grad_outw = totals[:, hid:] / ACCUM

    grad_part = lax.dot_general(
        grad_pre, w_in_full, (((1,), (1,)), ((), ())), preferred_element_type=jnp.float32
    )
    part_lo = grad_part[:, :half_width]
    part_hi = grad_part[:, half_width:]
    keep = jnp.where(core_index == 0, part_lo, part_hi)
    send = jnp.where(core_index == 0, part_hi, part_lo).astype(jnp.bfloat16)
    received = lax.ppermute(send, "llm", SWAP)
    grad_normed = keep + received.astype(jnp.float32)
    gain_half = lax.dynamic_slice_in_dim(norm_gain, core_index * half_width, half_width, 0)
    unit_half = lax.dynamic_slice_in_dim(unit, core_index * half_width, half_width, 1)
    grad_unit = grad_normed * gain_half
    sums = jnp.stack(
        [jnp.sum(grad_unit, axis=1), jnp.sum(grad_unit * unit_half, axis=1)], axis=1
    )
    sums = sums + lax.ppermute(sums, "llm", SWAP)
    mean_grad = sums[:, 0:1] / channels
    mean_cross = sums[:, 1:2] / channels
    grad_mixed = inv_std * (grad_unit - mean_grad - unit_half * mean_cross)
    kernel_half = lax.dynamic_slice_in_dim(kernel, core_index * half_width, half_width, 2)
    backward_half = depthwise(
        grad_mixed.reshape(-1, SIDE, SIDE, half_width), kernel_half[::-1, ::-1]
    ).reshape(row_count, half_width)
    grad_tiles = (mine_half.astype(jnp.float32) + backward_half).astype(jnp.bfloat16)
    return (grad_tiles, grad_in, grad_outw)


def x_width(mesh):
    group = mesh.devices[0, :, 0]
    try:
        return len({d.coords[0] for d in group})
    except (AttributeError, TypeError, IndexError):
        return 4


def solution(mesh):
    dp, fsdp, llm = mesh.devices.shape
    width = x_width(mesh)
    split = jax.sharding.Mesh(
        mesh.devices.reshape(dp, fsdp // width, width, llm), ("dp", "fy", "fx", "llm")
    )
    rows = ("dp", "fy", "fx")
    in_specs = (
        P(rows, None),
        P(rows, None),
        P(rows, None),
        P(rows, None),
        P(rows),
        P(),
        P(),
        P(),
        P(("fy", "fx"), "llm"),
        P(("fy", "fx"), "llm"),
    )
    out_specs = (P(rows, "llm"), P(rows, "llm"), P(rows, "llm"))
    return jax.shard_map(body, mesh=split, in_specs=in_specs, out_specs=out_specs, check_vma=False)
```

```python
import jax
import jax.numpy as jnp
from jax import lax
from jax.sharding import PartitionSpec as P

SIDE = 8
ACCUM = 64


def depthwise(images, kernel):
    return lax.conv_general_dilated(
        images,
        kernel[:, :, None, :],
        (1, 1),
        "SAME",
        dimension_numbers=("NHWC", "HWIO", "NHWC"),
        feature_group_count=images.shape[3],
        precision=lax.Precision.HIGHEST,
    )


def gelu_parts(hidden_in):
    cumulative = 0.5 * (1.0 + lax.erf(hidden_in * 0.7071067811865476))
    density = jnp.exp(-0.5 * hidden_in * hidden_in) * 0.3989422804014327
    return (hidden_in * cumulative, cumulative + hidden_in * density)


SWAP = [(0, 1), (1, 0)]


def body(
    tile_rows,
    grad_seq,
    visual_pos,
    assign,
    tile_count,
    kernel,
    norm_gain,
    layer_scale,
    weight_in,
    weight_out,
):
    groups = lax.axis_size("dp")
    height = lax.axis_size("fy")
    width = lax.axis_size("fx")
    shards = height * width
    row_count = tile_rows.shape[0]
    channels = tile_rows.shape[1]
    block_rows = row_count // groups
    half_width = channels // lax.axis_size("llm")
    core_index = lax.axis_index("llm")

    flat = (assign[0][:, None] * block_rows + jnp.arange(block_rows)[None, :]).reshape(row_count)
    chosen = flat[:, None] == jnp.arange(visual_pos.shape[1])[None, :]
    source_rows = jnp.sum(jnp.where(chosen, visual_pos, 0), axis=1)
    seq_half = lax.dynamic_slice_in_dim(grad_seq, core_index * half_width, half_width, 1)
    pick = source_rows[:, None] == jnp.arange(grad_seq.shape[0])[None, :]
    out_half = jnp.dot(
        pick.astype(seq_half.dtype), seq_half, preferred_element_type=jnp.float32
    ).astype(seq_half.dtype)
    arrived_half = lax.all_to_all(out_half, "dp", split_axis=0, concat_axis=0, tiled=True)
    present = jnp.arange(row_count) // (SIDE * SIDE) < tile_count[0]
    mine_half = jnp.where(present[:, None], arrived_half, jnp.zeros_like(arrived_half))
    other_half = lax.ppermute(mine_half, "llm", SWAP)
    first = jnp.where(core_index == 0, mine_half, other_half)
    second = jnp.where(core_index == 0, other_half, mine_half)
    grad_out = jnp.concatenate([first, second], axis=1)

    hid = weight_in.shape[1]
    both = jnp.concatenate([weight_in, weight_out], axis=1)
    y_block = lax.all_gather(both, "fy", axis=0)
    x_tiled = jnp.broadcast_to(y_block[:, None], (height, width) + both.shape)
    both_full = lax.all_to_all(x_tiled, "fx", split_axis=1, concat_axis=1, tiled=True).reshape(
        shards * both.shape[0], both.shape[1]
    )
    w_in_full = both_full[:, :hid]
    w_out_full = both_full[:, hid:]

    mixed = depthwise(
        tile_rows.astype(jnp.float32).reshape(-1, SIDE, SIDE, channels), kernel
    ).reshape(row_count, channels)
    row_mean = jnp.mean(mixed, axis=1, keepdims=True)
    centred = mixed - row_mean
    inv_std = lax.rsqrt(jnp.mean(centred * centred, axis=1, keepdims=True) + 1e-06)
    unit = centred * inv_std
    normed = (unit * norm_gain).astype(jnp.bfloat16)
    hidden_in = jnp.dot(normed, w_in_full, preferred_element_type=jnp.float32)
    activated, slope = gelu_parts(hidden_in)
    hidden = activated.astype(jnp.bfloat16)
    scaled = (grad_out.astype(jnp.float32) * layer_scale).astype(jnp.bfloat16)
    grad_hidden = jnp.dot(scaled, w_out_full, preferred_element_type=jnp.float32)
    grad_pre = (grad_hidden * slope).astype(jnp.bfloat16)

    term_in = lax.dot_general(
        normed, grad_pre, (((0,), (0,)), ((), ())), preferred_element_type=jnp.float32
    )
    term_out = lax.dot_general(
        scaled, hidden, (((0,), (0,)), ((), ())), preferred_element_type=jnp.float32
    )
    terms = jnp.concatenate([term_in, term_out], axis=1).astype(jnp.bfloat16)
    terms = terms.reshape(height, width, channels // shards, 2 * hid)
    x_parts = lax.all_to_all(terms, "fx", split_axis=1, concat_axis=1, tiled=True)
    x_sums = (jnp.sum(x_parts.astype(jnp.float32), axis=1) / ACCUM).astype(jnp.bfloat16)
    y_parts = lax.all_to_all(x_sums, "fy", split_axis=0, concat_axis=0, tiled=True)
    grad_in = jnp.sum(y_parts[:, :, :hid].astype(jnp.float32), axis=0)
    grad_outw = jnp.sum(y_parts[:, :, hid:].astype(jnp.float32), axis=0)

    grad_part = lax.dot_general(
        grad_pre, w_in_full, (((1,), (1,)), ((), ())), preferred_element_type=jnp.float32
    )
    part_lo = grad_part[:, :half_width]
    part_hi = grad_part[:, half_width:]
    keep = jnp.where(core_index == 0, part_lo, part_hi)
    send = jnp.where(core_index == 0, part_hi, part_lo).astype(jnp.bfloat16)
    received = lax.ppermute(send, "llm", SWAP)
    grad_normed = keep + received.astype(jnp.float32)
    gain_half = lax.dynamic_slice_in_dim(norm_gain, core_index * half_width, half_width, 0)
    unit_half = lax.dynamic_slice_in_dim(unit, core_index * half_width, half_width, 1)
    grad_unit = grad_normed * gain_half
    sums = jnp.stack(
        [jnp.sum(grad_unit, axis=1), jnp.sum(grad_unit * unit_half, axis=1)], axis=1
    )
    sums = sums + lax.ppermute(sums, "llm", SWAP)
    mean_grad = sums[:, 0:1] / channels
    mean_cross = sums[:, 1:2] / channels
    grad_mixed = inv_std * (grad_unit - mean_grad - unit_half * mean_cross)
    kernel_half = lax.dynamic_slice_in_dim(kernel, core_index * half_width, half_width, 2)
    backward_half = depthwise(
        grad_mixed.reshape(-1, SIDE, SIDE, half_width), kernel_half[::-1, ::-1]
    ).reshape(row_count, half_width)
    grad_tiles = (mine_half.astype(jnp.float32) + backward_half).astype(jnp.bfloat16)
    return (grad_tiles, grad_in, grad_outw)


def x_width(mesh):
    group = mesh.devices[0, :, 0]
    try:
        return len({d.coords[0] for d in group})
    except (AttributeError, TypeError, IndexError):
        return 4


def solution(mesh):
    dp, fsdp, llm = mesh.devices.shape
    width = x_width(mesh)
    split = jax.sharding.Mesh(
        mesh.devices.reshape(dp, fsdp // width, width, llm), ("dp", "fy", "fx", "llm")
    )
    rows = ("dp", "fy", "fx")
    in_specs = (
        P(rows, None),
        P(rows, None),
        P(rows, None),
        P(rows, None),
        P(rows),
        P(),
        P(),
        P(),
        P(("fy", "fx"), "llm"),
        P(("fy", "fx"), "llm"),
    )
    out_specs = (P(rows, "llm"), P(rows, "llm"), P(rows, "llm"))
    return jax.shard_map(body, mesh=split, in_specs=in_specs, out_specs=out_specs, check_vma=False)
```
